256 devices in a mesh: dp: 64 (over y, z, core), vocab: 4 (over x).
Axes of the slice: x: 4, y: 4, z: 8, core: 2. Of those that a mesh axis runs over, the one named last changes fastest.
Arguments:
- hidden_rows: bfloat16 [16384, 5120], P('dp'), may hold values from -300 to 300, as said below
- plan_lengths: int32 [64], replicated, may hold values from 1 to 256, 8192 in all
- shard_of_class: int32 [64], replicated, may hold values from 0 to 63, each once
- head_weight: bfloat16 [5120, 3072], P(None, 'vocab'), may hold values from -0.078125 to 0.078125
- teacher_logprobs: bfloat16 [8192, 3072], P('dp', 'vocab'), as said below
Outputs:
- row_grad: bfloat16 [16384, 5120], P('dp')
- row_kl: float32 [8192], P('dp')
The draws below stay inside these ranges and needn't reach their ends.
Inputs may be any that keep to these rules, and one draw needn't show every extreme that they name: `plan_lengths`: the plan lengths sum to 8192 and the longest is exactly 256. `shard_of_class`: each shard is named once. `hidden_rows`: unused slots hold finite values. `teacher_logprobs`: each row is a log-softmax over the 3072 entries, rounded to bfloat16.
All inputs are finite; a program needn't handle non-finite values.
Results may differ from the reference program's by a relative error of at most 0.0046.
Values may be sent and summed in bfloat16 or wider, within the bound.
No kernel may reach another device: no remote copies, remote signals or barrier semaphores. Data moves between devices by JAX's collectives and lax.ppermute only.
A program may use at most 64 MiB of HBM per device.

```python
import math
import jax
import jax.numpy as jnp
import numpy as np
from jax import lax

D = 5120
ROW_BAL = 128
SRC_CAP = 256
TOKENS = 8192
TOKENS_CAP = 16384
VOCAB = 3072
N_DP = 64


def draw_hidden_rows(key, part):
    first, second = jax.random.split(jax.random.fold_in(key, 11), 2)
    base = jnp.clip(jax.random.normal(first, (TOKENS_CAP, D), jnp.float32), -5.0, 5.0)
    scales = jnp.exp(jax.random.uniform(second, (TOKENS_CAP, 1), jnp.float32, 0.0, math.log(10.0)))
    values = base * scales
    return jnp.clip(values, -300.0, 300.0).astype(jnp.bfloat16)


def draw_teacher_logprobs(key, part):
    first = jax.random.fold_in(jax.random.fold_in(key, 23), 0)
    logits = 3.0 * jnp.clip(jax.random.normal(first, (TOKENS, VOCAB), jnp.float32), -6.0, 6.0)
    logprobs = logits - jax.scipy.special.logsumexp(logits, axis=1, keepdims=True)
    return logprobs.astype(jnp.bfloat16)


def block_scale(rng, shape, pieces, low, largest):
    def one(dim, shards_of):
        heights = jax.random.uniform(jax.random.fold_in(jax.random.fold_in(rng, 6), dim), (shards_of,), jnp.float32, low / len(pieces), largest / len(pieces))
        return jnp.repeat(jnp.exp(heights), shape[dim] // shards_of).reshape((-1,) + (1,) * (len(shape) - dim - 1))

    gain = one(*pieces[0])
    for cut in pieces[1:]:
        gain = gain * one(*cut)
    return gain


def length_profile(number_of, total, bound, slope):
    loads = [(1 << 20) // math.isqrt(standing ** slope) + 1 for standing in range(2, number_of + 1)]
    surplus, counts = total - bound - (number_of - 1), [1] * (number_of - 1)
    while surplus > 0:
        candidates = [i for i in range(number_of - 1) if counts[i] < bound]
        mass, budget = sum([loads[i] for i in candidates]), surplus
        for i in candidates:
            extra = min(bound - counts[i], max(1, budget * loads[i] // mass), surplus)
            counts[i] = counts[i] + extra
            surplus = surplus - extra
    return np.array([bound] + counts)


def ragged_sizes(key, number_of, total, bound, skew):
    if number_of == 2:
        one = jax.random.randint(key, (), max(1, total - bound), min(bound, total - 1) + 1)
        return jnp.stack([one, total - one])
    sizes = jnp.asarray(length_profile(number_of, total, bound, skew), jnp.int32)
    couples = (number_of - 1) // 2
    source_of, taker = sizes[1:1 + 2 * couples:2], sizes[2:2 + 2 * couples:2]
    margin = jnp.minimum(source_of - 1, bound - taker)
    passed = jax.random.randint(jax.random.fold_in(key, 1), (couples,), 0, 1 << 20) % (margin + 1)
    sizes = sizes.at[1:1 + 2 * couples:2].set(source_of - passed).at[2:2 + 2 * couples:2].set(taker + passed)
    return sizes[jax.random.permutation(jax.random.fold_in(key, 2), number_of)]


def gaussian(stream_key, dims, deviation, bound, cuts=(), kind=jnp.bfloat16):
    drawn = deviation * jax.random.normal(stream_key, dims, jnp.float32)
    if cuts:
        drawn = drawn * block_scale(stream_key, dims, cuts, -0.22, 0.18)
    return jnp.clip(drawn, -bound, bound).astype(kind)


def setup_inputs(seed: int = 0) -> dict:
    seeds = jax.random.split(jax.random.key(seed), 6)
    return {
        "hidden_rows": draw_hidden_rows(jax.random.fold_in(seeds[5], 71), 0),
        "plan_lengths": ragged_sizes(seeds[1], N_DP, TOKENS, SRC_CAP, 2).astype(jnp.int32),
        "shard_of_class": jax.random.permutation(seeds[2], N_DP).astype(jnp.int32),
        "head_weight": gaussian(seeds[3], (D, VOCAB), D ** -0.5, 0.078125, ((1, 4),)),
        "teacher_logprobs": draw_teacher_logprobs(jax.random.fold_in(seeds[5], 71), 0),
    }


loss_scale = 64.0


def divergence(row_block, teacher_block, weight):
    logits = jnp.dot(row_block, weight, preferred_element_type=jnp.float32)
    row_top = jnp.max(logits, axis=1, keepdims=True)
    log_total = row_top + jnp.log(jnp.sum(jnp.exp(logits - row_top), axis=1, keepdims=True))
    log_teacher = teacher_block.astype(jnp.float32)
    teacher_prob = jnp.exp(log_teacher)
    prob_total = jnp.sum(teacher_prob, axis=1, keepdims=True)
    row_div = jnp.sum(teacher_prob * (log_teacher - logits), axis=1) + prob_total[:, 0] * log_total[:, 0]
    grad_logits = (loss_scale * (prob_total * jnp.exp(logits - log_total) - teacher_prob)).astype(jnp.bfloat16)
    hidden_grad = jnp.dot(grad_logits, weight.T, preferred_element_type=jnp.float32).astype(jnp.bfloat16)
    return row_div, hidden_grad


def reference(hidden_rows, plan_lengths, shard_of_class, head_weight, teacher_logprobs):
    shards = N_DP
    lengths = plan_lengths.astype(jnp.int32)
    offsets = (jnp.cumsum(lengths) - lengths).astype(jnp.int32)
    classes = jnp.arange(shards, dtype=jnp.int32)
    inverse = jnp.sum(jnp.where(shard_of_class[None, :] == classes[:, None], classes[None, :], 0), axis=1).astype(jnp.int32)
    slot_index = jnp.arange(ROW_BAL, dtype=jnp.int32)

    def one_shard(shard_index):
        packed_index = (slot_index * shards + inverse[shard_index]).astype(jnp.int32)
        owner = (jnp.sum((offsets[None, :] <= packed_index[:, None]).astype(jnp.int32), axis=1) - 1).astype(jnp.int32)
        source_row = (owner * SRC_CAP + packed_index - offsets[owner]).astype(jnp.int32)
        row_block = hidden_rows[source_row]
        teacher_block = lax.dynamic_slice_in_dim(teacher_logprobs, (shard_index * ROW_BAL).astype(jnp.int32), ROW_BAL, 0)
        row_div, hidden_grad = divergence(row_block, teacher_block, head_weight)
        return row_div, hidden_grad, source_row

    row_divs, grads, source_rows = lax.map(one_shard, classes)
    row_kl = row_divs.reshape(-1)
    row_grad = jnp.zeros((TOKENS_CAP, D), jnp.bfloat16).at[source_rows.reshape(-1)].set(grads.reshape(-1, D))
    return row_grad, row_kl
```

```python
import jax
import jax.numpy as jnp
from jax import lax
from jax.sharding import PartitionSpec as P

loss_scale = 64.0


def divergence(row_block, teacher_block, live, weight):
    logits = jnp.dot(row_block, weight, preferred_element_type=jnp.float32)
    log_teacher = teacher_block.astype(jnp.float32)
    teacher_prob = jnp.exp(log_teacher)
    own_top = jnp.max(logits, axis=1)
    own_total = jnp.sum(jnp.exp(logits - own_top[:, None]), axis=1)
    own_mass = jnp.sum(teacher_prob, axis=1)
    own_cross = jnp.sum(teacher_prob * (log_teacher - logits), axis=1)
    stats = lax.all_gather(jnp.stack([own_top, own_total, own_mass, own_cross]), "vocab")
    tops, totals, masses, crosses = stats[:, 0], stats[:, 1], stats[:, 2], stats[:, 3]
    row_top = jnp.max(tops, axis=0)
    exp_total = jnp.sum(totals * jnp.exp(tops - row_top[None, :]), axis=0)
    prob_total = jnp.sum(masses, axis=0)
    cross_term = jnp.sum(crosses, axis=0)
    log_total = row_top + jnp.log(exp_total)
    row_div = jnp.where(live, cross_term + prob_total * log_total, 0.0)
    grad_logits = jnp.where(
        live[:, None],
        loss_scale * (prob_total[:, None] * jnp.exp(logits - log_total[:, None]) - teacher_prob),
        0.0,
    ).astype(jnp.bfloat16)
    partial_grad = lax.dot_general(
        grad_logits, weight, (((1,), (1,)), ((), ())), preferred_element_type=jnp.float32
    )
    summed = lax.psum_scatter(partial_grad, "vocab", scatter_dimension=0, tiled=True)
    hidden_grad = lax.all_gather(summed.astype(jnp.bfloat16), "vocab", axis=0, tiled=True)
    return hidden_grad, row_div


def body(hidden_rows, plan_lengths, shard_of_class, head_weight, teacher_logprobs):
    shards = lax.axis_size("dp")
    myself = lax.axis_index("dp")
    source_slots = hidden_rows.shape[0]
    slot_depth = source_slots // shards
    balanced = teacher_logprobs.shape[0]
    offsets = jnp.cumsum(plan_lengths) - plan_lengths
    classes = jnp.arange(shards, dtype=jnp.int32)
    inverse = jnp.sum(
        jnp.where(shard_of_class[None, :] == classes[:, None], classes[None, :], 0), axis=1
    )
    depth = jnp.arange(slot_depth, dtype=jnp.int32)
    first_col = (inverse[myself] - offsets) % shards
    first_slot = (offsets + first_col) // shards
    send_rows = jnp.minimum(first_slot[:, None] + depth[None, :], balanced - 1)
    outgoing = jnp.take(teacher_logprobs, send_rows.reshape(-1), axis=0).reshape(
        shards, slot_depth, teacher_logprobs.shape[1]
    )
    arriving = lax.all_to_all(outgoing, "dp", split_axis=0, concat_axis=0, tiled=True)
    own_offset = offsets[myself]
    shard_at = shard_of_class[(own_offset + classes) % shards]
    teacher_slots = jnp.take(arriving, shard_at, axis=0)
    teacher_slots = jnp.transpose(teacher_slots, (1, 0, 2)).reshape(source_slots, -1)
    live = jnp.arange(source_slots, dtype=jnp.int32) < plan_lengths[myself]
    row_grad, row_div = divergence(hidden_rows, teacher_slots, live, head_weight)
    every_div = lax.all_gather(row_div, "dp")
    packed = jnp.arange(balanced, dtype=jnp.int32) * shards + inverse[myself]
    owner = jnp.sum((offsets[None, :] <= packed[:, None]).astype(jnp.int32), axis=1) - 1
    row_kl = every_div[owner, packed - offsets[owner]]
    return row_grad, row_kl


def solution(mesh):
    return jax.shard_map(
        body,
        mesh=mesh,
        in_specs=(P("dp", None), P(), P(), P(None, "vocab"), P("dp", "vocab")),
        out_specs=(P("dp", None), P("dp")),
        check_vma=False,
    )
```

```python
import jax
import jax.numpy as jnp
from jax import lax
from jax.sharding import PartitionSpec as P

loss_scale = 64.0


def divergence(row_block, teacher_block, live, weight):
    logits = jnp.dot(row_block, weight, preferred_element_type=jnp.float32)
    log_teacher = teacher_block.astype(jnp.float32)
    teacher_prob = jnp.exp(log_teacher)
    own_top = jnp.max(logits, axis=1)
    own_total = jnp.sum(jnp.exp(logits - own_top[:, None]), axis=1)
    own_mass = jnp.sum(teacher_prob, axis=1)
    own_cross = jnp.sum(teacher_prob * (log_teacher - logits), axis=1)
    stats = lax.all_gather(jnp.stack([own_top, own_total, own_mass, own_cross]), "vocab")
    tops, totals, masses, crosses = stats[:, 0], stats[:, 1], stats[:, 2], stats[:, 3]
    row_top = jnp.max(tops, axis=0)
    exp_total = jnp.sum(totals * jnp.exp(tops - row_top[None, :]), axis=0)
    prob_total = jnp.sum(masses, axis=0)
    cross_term = jnp.sum(crosses, axis=0)
    log_total = row_top + jnp.log(exp_total)
    row_div = jnp.where(live, cross_term + prob_total * log_total, 0.0)
    grad_logits = jnp.where(
        live[:, None],
        loss_scale * (prob_total[:, None] * jnp.exp(logits - log_total[:, None]) - teacher_prob),
        0.0,
    ).astype(jnp.bfloat16)
    partial_grad = lax.dot_general(
        grad_logits, weight, (((1,), (1,)), ((), ())), preferred_element_type=jnp.float32
    )
    summed = lax.psum_scatter(partial_grad, "vocab", scatter_dimension=0, tiled=True)
    hidden_grad = lax.all_gather(summed.astype(jnp.bfloat16), "vocab", axis=0, tiled=True)
    return hidden_grad, row_div


def body(hidden_rows, plan_lengths, shard_of_class, head_weight, teacher_logprobs):
    shards = lax.axis_size("dp")
    myself = lax.axis_index("dp")
    source_slots = hidden_rows.shape[0]
    slot_depth = source_slots // shards
    balanced = teacher_logprobs.shape[0]
    offsets = jnp.cumsum(plan_lengths) - plan_lengths
    classes = jnp.arange(shards, dtype=jnp.int32)
    inverse = jnp.sum(
        jnp.where(shard_of_class[None, :] == classes[:, None], classes[None, :], 0), axis=1
    )
    depth = jnp.arange(slot_depth, dtype=jnp.int32)
    first_col = (inverse[myself] - offsets) % shards
    first_slot = (offsets + first_col) // shards
    send_rows = jnp.minimum(first_slot[:, None] + depth[None, :], balanced - 1)
    outgoing = jnp.take(teacher_logprobs, send_rows.reshape(-1), axis=0).reshape(
        shards, slot_depth, teacher_logprobs.shape[1]
    )
    arriving = lax.all_to_all(outgoing, "dp", split_axis=0, concat_axis=0, tiled=True)
    own_offset = offsets[myself]
    shard_at = shard_of_class[(own_offset + classes) % shards]
    teacher_slots = jnp.take(arriving, shard_at, axis=0)
    teacher_slots = jnp.transpose(teacher_slots, (1, 0, 2)).reshape(source_slots, -1)
    live = jnp.arange(source_slots, dtype=jnp.int32) < plan_lengths[myself]
    row_grad, row_div = divergence(hidden_rows, teacher_slots, live, head_weight)
    column_of = (inverse - own_offset) % shards
    div_out = jnp.take(row_div.reshape(slot_depth, shards), column_of, axis=1).T
    div_in = lax.all_to_all(div_out, "dp", split_axis=0, concat_axis=0, tiled=True)
    packed = jnp.arange(balanced, dtype=jnp.int32) * shards + inverse[myself]
    owner = jnp.sum((offsets[None, :] <= packed[:, None]).astype(jnp.int32), axis=1) - 1
    row_kl = div_in[owner, (packed - offsets[owner]) // shards]
    return row_grad, row_kl


def solution(mesh):
    return jax.shard_map(
        body,
        mesh=mesh,
        in_specs=(P("dp", None), P(), P(), P(None, "vocab"), P("dp", "vocab")),
        out_specs=(P("dp", None), P("dp")),
        check_vma=False,
    )
```

```python
import jax
import jax.numpy as jnp
from jax import lax
from jax.sharding import PartitionSpec as P

loss_scale = 64.0


def divergence(row_block, teacher_block, live, weight):
    logits = jnp.dot(row_block, weight, preferred_element_type=jnp.float32)
    log_teacher = teacher_block.astype(jnp.float32)
    teacher_prob = jnp.exp(log_teacher)
    own_top = jnp.max(logits, axis=1)
    own_total = jnp.sum(jnp.exp(logits - own_top[:, None]), axis=1)
    own_mass = jnp.sum(teacher_prob, axis=1)
    own_cross = jnp.sum(teacher_prob * (log_teacher - logits), axis=1)
    stats = lax.all_gather(jnp.stack([own_top, own_total, own_mass, own_cross]), "vocab")
    tops, totals, masses, crosses = stats[:, 0], stats[:, 1], stats[:, 2], stats[:, 3]
    row_top = jnp.max(tops, axis=0)
    exp_total = jnp.sum(totals * jnp.exp(tops - row_top[None, :]), axis=0)
    prob_total = jnp.sum(masses, axis=0)
    cross_term = jnp.sum(crosses, axis=0)
    log_total = row_top + jnp.log(exp_total)
    row_div = jnp.where(live, cross_term + prob_total * log_total, 0.0)
    grad_logits = jnp.where(
        live[:, None],
        loss_scale * (prob_total[:, None] * jnp.exp(logits - log_total[:, None]) - teacher_prob),
        0.0,
    ).astype(jnp.bfloat16)
    partial_grad = lax.dot_general(
        grad_logits, weight, (((1,), (1,)), ((), ())), preferred_element_type=jnp.float32
    )
    hidden_grad = ring_all_reduce(partial_grad)
    return hidden_grad, row_div


def ring_all_reduce(partial):
    ring = lax.axis_size("vocab")
    me = lax.axis_index("vocab")
    rows, width = partial.shape
    chunk = rows // (2 * ring)
    halves = partial.reshape(2, ring, chunk, width)
    forward = [(i, (i + 1) % ring) for i in range(ring)]
    backward = [(i, (i - 1) % ring) for i in range(ring)]

    def own(half, index):
        return lax.dynamic_index_in_dim(halves[half], index % ring, 0, keepdims=False)

    up = own(0, me - 1)
    down = own(1, me + 1)
    for step in range(ring - 1):
        up = lax.ppermute(up, "vocab", forward) + own(0, me - step - 2)
        down = lax.ppermute(down, "vocab", backward) + own(1, me + step + 2)
    up = up.astype(jnp.bfloat16)
    down = down.astype(jnp.bfloat16)
    ups, downs = [up], [down]
    for step in range(ring - 1):
        up = lax.ppermute(up, "vocab", forward)
        down = lax.ppermute(down, "vocab", backward)
        ups.append(up)
        downs.append(down)
    ups = jnp.stack(ups)
    downs = jnp.stack(downs)
    order = jnp.arange(ring, dtype=jnp.int32)
    top = jnp.take(ups, (me - order) % ring, axis=0)
    bottom = jnp.take(downs, (order - me) % ring, axis=0)
    return jnp.concatenate([top, bottom], axis=0).reshape(rows, width)


def body(hidden_rows, plan_lengths, shard_of_class, head_weight, teacher_logprobs):
    shards = lax.axis_size("dp")
    myself = lax.axis_index("dp")
    source_slots = hidden_rows.shape[0]
    slot_depth = source_slots // shards
    balanced = teacher_logprobs.shape[0]
    offsets = jnp.cumsum(plan_lengths) - plan_lengths
    classes = jnp.arange(shards, dtype=jnp.int32)
    inverse = jnp.sum(
        jnp.where(shard_of_class[None, :] == classes[:, None], classes[None, :], 0), axis=1
    )
    depth = jnp.arange(slot_depth, dtype=jnp.int32)
    first_col = (inverse[myself] - offsets) % shards
    first_slot = (offsets + first_col) // shards
    send_rows = jnp.minimum(first_slot[:, None] + depth[None, :], balanced - 1)
    outgoing = jnp.take(teacher_logprobs, send_rows.reshape(-1), axis=0).reshape(
        shards, slot_depth, teacher_logprobs.shape[1]
    )
    arriving = lax.all_to_all(outgoing, "dp", split_axis=0, concat_axis=0, tiled=True)
    own_offset = offsets[myself]
    shard_at = shard_of_class[(own_offset + classes) % shards]
    teacher_slots = jnp.take(arriving, shard_at, axis=0)
    teacher_slots = jnp.transpose(teacher_slots, (1, 0, 2)).reshape(source_slots, -1)
    live = jnp.arange(source_slots, dtype=jnp.int32) < plan_lengths[myself]
    row_grad, row_div = divergence(hidden_rows, teacher_slots, live, head_weight)
    column_of = (inverse - own_offset) % shards
    div_out = jnp.take(row_div.reshape(slot_depth, shards), column_of, axis=1).T
    div_in = lax.all_to_all(div_out, "dp", split_axis=0, concat_axis=0, tiled=True)
    packed = jnp.arange(balanced, dtype=jnp.int32) * shards + inverse[myself]
    owner = jnp.sum((offsets[None, :] <= packed[:, None]).astype(jnp.int32), axis=1) - 1
    row_kl = div_in[owner, (packed - offsets[owner]) // shards]
    return row_grad, row_kl


def solution(mesh):
    return jax.shard_map(
        body,
        mesh=mesh,
        in_specs=(P("dp", None), P(), P(), P(None, "vocab"), P("dp", "vocab")),
        out_specs=(P("dp", None), P("dp")),
        check_vma=False,
    )
```

```python
import jax
import jax.numpy as jnp
from jax import lax
from jax.sharding import PartitionSpec as P

loss_scale = 64.0


def divergence(row_block, teacher_block, live, weight):
    logits = jnp.dot(row_block, weight, preferred_element_type=jnp.float32)
    log_teacher = teacher_block.astype(jnp.float32)
    teacher_prob = jnp.exp(log_teacher)
    own_top = jnp.max(logits, axis=1)
    own_total = jnp.sum(jnp.exp(logits - own_top[:, None]), axis=1)
    own_mass = jnp.sum(teacher_prob, axis=1)
    own_cross = jnp.sum(teacher_prob * (log_teacher - logits), axis=1)
    stats = lax.all_gather(jnp.stack([own_top, own_total, own_mass, own_cross]), "vocab")
    tops, totals, masses, crosses = stats[:, 0], stats[:, 1], stats[:, 2], stats[:, 3]
    row_top = jnp.max(tops, axis=0)
    exp_total = jnp.sum(totals * jnp.exp(tops - row_top[None, :]), axis=0)
    prob_total = jnp.sum(masses, axis=0)
    cross_term = jnp.sum(crosses, axis=0)
    log_total = row_top + jnp.log(exp_total)
    row_div = jnp.where(live, cross_term + prob_total * log_total, 0.0)
    grad_logits = jnp.where(
        live[:, None],
        loss_scale * (prob_total[:, None] * jnp.exp(logits - log_total[:, None]) - teacher_prob),
        0.0,
    ).astype(jnp.bfloat16)
    partial_grad = lax.dot_general(
        grad_logits, weight, (((1,), (1,)), ((), ())), preferred_element_type=jnp.float32
    )
    hidden_grad = ring_all_reduce(partial_grad)
    return hidden_grad, row_div


def ring_all_reduce(partial):
    ring = lax.axis_size("vocab")
    me = lax.axis_index("vocab")
    rows, width = partial.shape
    chunk = rows // (2 * ring)
    halves = partial.reshape(2, ring, chunk, width)
    forward = [(i, (i + 1) % ring) for i in range(ring)]
    backward = [(i, (i - 1) % ring) for i in range(ring)]

    def own(half, index):
        return lax.dynamic_index_in_dim(halves[half], index % ring, 0, keepdims=False)

    up = own(0, me - 1)
    down = own(1, me + 1)
    for step in range(ring - 1):
        up = lax.ppermute(up, "vocab", forward) + own(0, me - step - 2)
        down = lax.ppermute(down, "vocab", backward) + own(1, me + step + 2)
    up = up.astype(jnp.bfloat16)
    down = down.astype(jnp.bfloat16)
    ups, downs = [up], [down]
    for step in range(ring - 1):
        up = lax.ppermute(up, "vocab", forward)
        down = lax.ppermute(down, "vocab", backward)
        ups.append(up)
        downs.append(down)
    placed = jnp.zeros((2 * ring, chunk, width), jnp.bfloat16)
    for k in range(ring):
        placed = lax.dynamic_update_index_in_dim(placed, ups[k], (me - k) % ring, 0)
        placed = lax.dynamic_update_index_in_dim(placed, downs[k], ring + (me + k) % ring, 0)
    return placed.reshape(rows, width)


def body(hidden_rows, plan_lengths, shard_of_class, head_weight, teacher_logprobs):
    shards = lax.axis_size("dp")
    myself = lax.axis_index("dp")
    source_slots = hidden_rows.shape[0]
    slot_depth = source_slots // shards
    balanced = teacher_logprobs.shape[0]
    offsets = jnp.cumsum(plan_lengths) - plan_lengths
    classes = jnp.arange(shards, dtype=jnp.int32)
    inverse = jnp.sum(
        jnp.where(shard_of_class[None, :] == classes[:, None], classes[None, :], 0), axis=1
    )
    depth = jnp.arange(slot_depth, dtype=jnp.int32)
    first_col = (inverse[myself] - offsets) % shards
    first_slot = (offsets + first_col) // shards
    send_rows = jnp.minimum(first_slot[:, None] + depth[None, :], balanced - 1)
    outgoing = jnp.take(teacher_logprobs, send_rows.reshape(-1), axis=0).reshape(
        shards, slot_depth, teacher_logprobs.shape[1]
    )
    arriving = lax.all_to_all(outgoing, "dp", split_axis=0, concat_axis=0, tiled=True)
    own_offset = offsets[myself]
    shard_at = shard_of_class[(own_offset + classes) % shards]
    teacher_slots = jnp.take(arriving, shard_at, axis=0)
    teacher_slots = jnp.transpose(teacher_slots, (1, 0, 2)).reshape(source_slots, -1)
    live = jnp.arange(source_slots, dtype=jnp.int32) < plan_lengths[myself]
    row_grad, row_div = divergence(hidden_rows, teacher_slots, live, head_weight)
    slot_class = (own_offset + jnp.arange(source_slots, dtype=jnp.int32)) % shards
    slot_target = shard_of_class[slot_class] * balanced + (own_offset + jnp.arange(source_slots, dtype=jnp.int32)) // shards
    slot_target = jnp.where(live, slot_target, shards * balanced)
    positions = jnp.arange(shards * balanced, dtype=jnp.int32)
    column_of = (inverse - own_offset) % shards
    target_of = jnp.take(slot_target.reshape(slot_depth, shards), column_of, axis=1)
    div_of = jnp.take(row_div.reshape(slot_depth, shards), column_of, axis=1)
    spread = jnp.zeros((shards, balanced), jnp.float32)
    for r in range(slot_depth):
        hit = target_of[r][:, None] == positions.reshape(shards, balanced)
        spread = spread + jnp.where(hit, div_of[r][:, None], 0.0)
    wide = jnp.broadcast_to(spread[:, :, None], (shards, balanced, 16))
    row_kl = lax.psum_scatter(wide, "dp", scatter_dimension=0, tiled=True)[0, :, 0]
    return row_grad, row_kl


def solution(mesh):
    return jax.shard_map(
        body,
        mesh=mesh,
        in_specs=(P("dp", None), P(), P(), P(None, "vocab"), P("dp", "vocab")),
        out_specs=(P("dp", None), P("dp")),
        check_vma=False,
    )
```

```python
import jax
import jax.numpy as jnp
from jax import lax
from jax.sharding import PartitionSpec as P

loss_scale = 64.0


def divergence(row_block, teacher_block, live, weight):
    logits = jnp.dot(row_block, weight, preferred_element_type=jnp.float32)
    log_teacher = teacher_block.astype(jnp.float32)
    teacher_prob = jnp.exp(log_teacher)
    own_top = jnp.max(logits, axis=1)
    own_total = jnp.sum(jnp.exp(logits - own_top[:, None]), axis=1)
    own_mass = jnp.sum(teacher_prob, axis=1)
    own_cross = jnp.sum(teacher_prob * (log_teacher - logits), axis=1)
    stats = lax.all_gather(jnp.stack([own_top, own_total, own_mass, own_cross]), "vocab")
    tops, totals, masses, crosses = stats[:, 0], stats[:, 1], stats[:, 2], stats[:, 3]
    row_top = jnp.max(tops, axis=0)
    exp_total = jnp.sum(totals * jnp.exp(tops - row_top[None, :]), axis=0)
    prob_total = jnp.sum(masses, axis=0)
    cross_term = jnp.sum(crosses, axis=0)
    log_total = row_top + jnp.log(exp_total)
    row_div = jnp.where(live, cross_term + prob_total * log_total, 0.0)
    grad_logits = jnp.where(
        live[:, None],
        loss_scale * (prob_total[:, None] * jnp.exp(logits - log_total[:, None]) - teacher_prob),
        0.0,
    ).astype(jnp.bfloat16)
    partial_grad = lax.dot_general(
        grad_logits, weight, (((1,), (1,)), ((), ())), preferred_element_type=jnp.float32
    )
    hidden_grad = ring_all_reduce(partial_grad)
    return hidden_grad, row_div


def ring_all_reduce(partial):
    ring = lax.axis_size("vocab")
    me = lax.axis_index("vocab")
    rows, width = partial.shape
    chunk = rows // (2 * ring)
    halves = partial.reshape(2, ring, chunk, width)
    forward = [(i, (i + 1) % ring) for i in range(ring)]
    backward = [(i, (i - 1) % ring) for i in range(ring)]

    def own(half, index):
        return lax.dynamic_index_in_dim(halves[half], index % ring, 0, keepdims=False)

    up = own(0, me - 1)
    down = own(1, me + 1)
    for step in range(ring - 1):
        up = lax.ppermute(up, "vocab", forward)
        down = lax.ppermute(down, "vocab", backward)
        up = up + own(0, me - step - 2)
        down = down + own(1, me + step + 2)
    up = up.astype(jnp.bfloat16)
    down = down.astype(jnp.bfloat16)
    ups, downs = [up], [down]
    for _ in range(ring - 1):
        up = lax.ppermute(up, "vocab", forward)
        down = lax.ppermute(down, "vocab", backward)
        ups.append(up)
        downs.append(down)
    placed = jnp.zeros((2 * ring, chunk, width), jnp.bfloat16)
    for k in range(ring):
        placed = lax.dynamic_update_index_in_dim(placed, ups[k], (me - k) % ring, 0)
        placed = lax.dynamic_update_index_in_dim(placed, downs[k], ring + (me + k) % ring, 0)
    return placed.reshape(rows, width)


def body(hidden_rows, plan_lengths, shard_of_class, head_weight, teacher_logprobs):
    shards = lax.axis_size("dp")
    myself = lax.axis_index("dp")
    source_slots = hidden_rows.shape[0]
    slot_depth = source_slots // shards
    balanced = teacher_logprobs.shape[0]
    offsets = jnp.cumsum(plan_lengths) - plan_lengths
    classes = jnp.arange(shards, dtype=jnp.int32)
    inverse = jnp.sum(
        jnp.where(shard_of_class[None, :] == classes[:, None], classes[None, :], 0), axis=1
    )
    depth = jnp.arange(slot_depth, dtype=jnp.int32)
    first_col = (inverse[myself] - offsets) % shards
    first_slot = (offsets + first_col) // shards
    send_rows = jnp.minimum(first_slot[:, None] + depth[None, :], balanced - 1)
    outgoing = jnp.take(teacher_logprobs, send_rows.reshape(-1), axis=0).reshape(
        shards, slot_depth, teacher_logprobs.shape[1]
    )
    arriving = lax.all_to_all(outgoing, "dp", split_axis=0, concat_axis=0, tiled=True)
    own_offset = offsets[myself]
    shard_at = shard_of_class[(own_offset + classes) % shards]
    teacher_slots = jnp.take(arriving, shard_at, axis=0)
    teacher_slots = jnp.transpose(teacher_slots, (1, 0, 2)).reshape(source_slots, -1)
    live = jnp.arange(source_slots, dtype=jnp.int32) < plan_lengths[myself]
    row_grad, row_div = divergence(hidden_rows, teacher_slots, live, head_weight)
    column_of = (inverse - own_offset) % shards
    div_out = jnp.take(row_div.reshape(slot_depth, shards), column_of, axis=1).T
    div_in = lax.all_to_all(div_out, "dp", split_axis=0, concat_axis=0, tiled=True)
    packed = jnp.arange(balanced, dtype=jnp.int32) * shards + inverse[myself]
    owner = jnp.sum((offsets[None, :] <= packed[:, None]).astype(jnp.int32), axis=1) - 1
    row_kl = div_in[owner, (packed - offsets[owner]) // shards]
    return row_grad, row_kl


def solution(mesh):
    return jax.shard_map(
        body,
        mesh=mesh,
        in_specs=(P("dp", None), P(), P(), P(None, "vocab"), P("dp", "vocab")),
        out_specs=(P("dp", None), P("dp")),
        check_vma=False,
    )
```

```python
import jax
import jax.numpy as jnp
from jax import lax
from jax.sharding import PartitionSpec as P

loss_scale = 64.0


def divergence(row_block, teacher_block, live, weight):
    logits = jnp.dot(row_block, weight, preferred_element_type=jnp.float32)
    log_teacher = teacher_block.astype(jnp.float32)
    teacher_prob = jnp.exp(log_teacher)
    own_top = jnp.max(logits, axis=1)
    own_total = jnp.sum(jnp.exp(logits - own_top[:, None]), axis=1)
    own_mass = jnp.sum(teacher_prob, axis=1)
    own_cross = jnp.sum(teacher_prob * (log_teacher - logits), axis=1)
    mine = lax.axis_index("vocab") == jnp.arange(lax.axis_size("vocab"), dtype=jnp.int32)
    local = jnp.stack([own_top, own_total, own_mass, own_cross])
    stats = lax.psum(jnp.where(mine[:, None, None], local[None], 0.0), "vocab")
    tops, totals, masses, crosses = stats[:, 0], stats[:, 1], stats[:, 2], stats[:, 3]
    row_top = jnp.max(tops, axis=0)
    exp_total = jnp.sum(totals * jnp.exp(tops - row_top[None, :]), axis=0)
    prob_total = jnp.sum(masses, axis=0)
    cross_term = jnp.sum(crosses, axis=0)
    log_total = row_top + jnp.log(exp_total)
    row_div = jnp.where(live, cross_term + prob_total * log_total, 0.0)
    grad_logits = jnp.where(
        live[:, None],
        loss_scale * (prob_total[:, None] * jnp.exp(logits - log_total[:, None]) - teacher_prob),
        0.0,
    ).astype(jnp.bfloat16)
    partial_grad = lax.dot_general(
        grad_logits, weight, (((1,), (1,)), ((), ())), preferred_element_type=jnp.float32
    )
    hidden_grad = ring_all_reduce(partial_grad)
    return hidden_grad, row_div


def ring_all_reduce(partial):
    ring = lax.axis_size("vocab")
    me = lax.axis_index("vocab")
    rows, width = partial.shape
    chunk = rows // (2 * ring)
    halves = partial.reshape(2, ring, chunk, width)
    forward = [(i, (i + 1) % ring) for i in range(ring)]
    backward = [(i, (i - 1) % ring) for i in range(ring)]

    def own(half, index):
        return lax.dynamic_index_in_dim(halves[half], index % ring, 0, keepdims=False)

    up = own(0, me - 1)
    down = own(1, me + 1)
    for step in range(ring - 1):
        up = lax.ppermute(up, "vocab", forward)
        down = lax.ppermute(down, "vocab", backward)
        up = up + own(0, me - step - 2)
        down = down + own(1, me + step + 2)
    up = up.astype(jnp.bfloat16)
    down = down.astype(jnp.bfloat16)
    ups, downs = [up], [down]
    for _ in range(ring - 1):
        up = lax.ppermute(up, "vocab", forward)
        down = lax.ppermute(down, "vocab", backward)
        ups.append(up)
        downs.append(down)
    placed = jnp.zeros((2 * ring, chunk, width), jnp.bfloat16)
    for k in range(ring):
        placed = lax.dynamic_update_index_in_dim(placed, ups[k], (me - k) % ring, 0)
        placed = lax.dynamic_update_index_in_dim(placed, downs[k], ring + (me + k) % ring, 0)
    return placed.reshape(rows, width)


def body(hidden_rows, plan_lengths, shard_of_class, head_weight, teacher_logprobs):
    shards = lax.axis_size("dp")
    myself = lax.axis_index("dp")
    source_slots = hidden_rows.shape[0]
    slot_depth = source_slots // shards
    balanced = teacher_logprobs.shape[0]
    offsets = jnp.cumsum(plan_lengths) - plan_lengths
    classes = jnp.arange(shards, dtype=jnp.int32)
    inverse = jnp.sum(
        jnp.where(shard_of_class[None, :] == classes[:, None], classes[None, :], 0), axis=1
    )
    depth = jnp.arange(slot_depth, dtype=jnp.int32)
    first_col = (inverse[myself] - offsets) % shards
    first_slot = (offsets + first_col) // shards
    send_rows = jnp.minimum(first_slot[:, None] + depth[None, :], balanced - 1)
    outgoing = jnp.take(teacher_logprobs, send_rows.reshape(-1), axis=0, mode="clip").reshape(
        shards, slot_depth, teacher_logprobs.shape[1]
    )
    arriving = lax.all_to_all(outgoing, "dp", split_axis=0, concat_axis=0, tiled=True)
    own_offset = offsets[myself]
    shard_at = shard_of_class[(own_offset + classes) % shards]
    teacher_slots = jnp.take(arriving, shard_at, axis=0, mode="clip")
    teacher_slots = jnp.transpose(teacher_slots, (1, 0, 2)).reshape(source_slots, -1)
    live = jnp.arange(source_slots, dtype=jnp.int32) < plan_lengths[myself]
    row_grad, row_div = divergence(hidden_rows, teacher_slots, live, head_weight)
    column_of = (inverse - own_offset) % shards
    div_out = jnp.take(row_div.reshape(slot_depth, shards), column_of, axis=1, mode="clip").T
    div_in = lax.all_to_all(div_out, "dp", split_axis=0, concat_axis=0, tiled=True)
    packed = jnp.arange(balanced, dtype=jnp.int32) * shards + inverse[myself]
    owner = jnp.sum((offsets[None, :] <= packed[:, None]).astype(jnp.int32), axis=1) - 1
    row_kl = div_in[owner, (packed - offsets[owner]) // shards]
    return row_grad, row_kl


def solution(mesh):
    return jax.shard_map(
        body,
        mesh=mesh,
        in_specs=(P("dp", None), P(), P(), P(None, "vocab"), P("dp", "vocab")),
        out_specs=(P("dp", None), P("dp")),
        check_vma=False,
    )
```

```python
import jax
import jax.numpy as jnp
from jax import lax
from jax.sharding import PartitionSpec as P

loss_scale = 64.0


def divergence(row_block, teacher_block, live, weight):
    logits = jnp.dot(row_block, weight, preferred_element_type=jnp.float32)
    log_teacher = teacher_block.astype(jnp.float32)
    teacher_prob = jnp.exp(log_teacher)
    own_top = jnp.max(logits, axis=1)
    own_total = jnp.sum(jnp.exp(logits - own_top[:, None]), axis=1)
    own_mass = jnp.sum(teacher_prob, axis=1)
    own_cross = jnp.sum(teacher_prob * (log_teacher - logits), axis=1)
    stats = lax.all_gather(jnp.stack([own_top, own_total, own_mass, own_cross]), "vocab")
    tops, totals, masses, crosses = stats[:, 0], stats[:, 1], stats[:, 2], stats[:, 3]
    row_top = jnp.max(tops, axis=0)
    exp_total = jnp.sum(totals * jnp.exp(tops - row_top[None, :]), axis=0)
    prob_total = jnp.sum(masses, axis=0)
    cross_term = jnp.sum(crosses, axis=0)
    log_total = row_top + jnp.log(exp_total)
    row_div = jnp.where(live, cross_term + prob_total * log_total, 0.0)
    grad_logits = jnp.where(
        live[:, None],
        loss_scale * (prob_total[:, None] * jnp.exp(logits - log_total[:, None]) - teacher_prob),
        0.0,
    ).astype(jnp.bfloat16)
    partial_grad = lax.dot_general(
        grad_logits, weight, (((1,), (1,)), ((), ())), preferred_element_type=jnp.float32
    )
    hidden_grad = ring_all_reduce(partial_grad)
    return hidden_grad, row_div


def ring_all_reduce(partial):
    ring = lax.axis_size("vocab")
    me = lax.axis_index("vocab")
    rows, width = partial.shape
    chunk = rows // (2 * ring)
    halves = partial.reshape(2, ring, chunk, width)
    forward = [(i, (i + 1) % ring) for i in range(ring)]
    backward = [(i, (i - 1) % ring) for i in range(ring)]

    def own(half, index):
        return lax.dynamic_index_in_dim(halves[half], index % ring, 0, keepdims=False)

    up = own(0, me - 1)
    down = own(1, me + 1)
    for step in range(ring - 1):
        up = lax.ppermute(up, "vocab", forward)
        down = lax.ppermute(down, "vocab", backward)
        up = up + own(0, me - step - 2)
        down = down + own(1, me + step + 2)
    up = up.astype(jnp.bfloat16)
    down = down.astype(jnp.bfloat16)
    ups, downs = [up], [down]
    for _ in range(ring - 1):
        up = lax.ppermute(up, "vocab", forward)
        down = lax.ppermute(down, "vocab", backward)
        ups.append(up)
        downs.append(down)
    placed = jnp.zeros((2 * ring, chunk, width), jnp.bfloat16)
    for k in range(ring):
        placed = lax.dynamic_update_index_in_dim(placed, ups[k], (me - k) % ring, 0)
        placed = lax.dynamic_update_index_in_dim(placed, downs[k], ring + (me + k) % ring, 0)
    return placed.reshape(rows, width)


def body(hidden_rows, plan_lengths, shard_of_class, head_weight, teacher_logprobs):
    shards = lax.axis_size("dp")
    myself = lax.axis_index("dp")
    source_slots = hidden_rows.shape[0]
    slot_depth = source_slots // shards
    balanced = teacher_logprobs.shape[0]
    offsets = jnp.cumsum(plan_lengths) - plan_lengths
    classes = jnp.arange(shards, dtype=jnp.int32)
    inverse = jnp.sum(
        jnp.where(shard_of_class[None, :] == classes[:, None], classes[None, :], 0), axis=1
    )
    depth = jnp.arange(slot_depth, dtype=jnp.int32)
    first_col = (inverse[myself] - offsets) % shards
    first_slot = (offsets + first_col) // shards
    send_rows = jnp.minimum(first_slot[:, None] + depth[None, :], balanced - 1)
    outgoing = jnp.take(teacher_logprobs, send_rows, axis=0, mode="clip")
    arriving = lax.all_to_all(outgoing, "dp", split_axis=0, concat_axis=0, tiled=True)
    own_offset = offsets[myself]
    shard_at = shard_of_class[(own_offset + classes) % shards]
    teacher_slots = jnp.take(arriving, shard_at, axis=0, mode="clip")
    teacher_slots = jnp.transpose(teacher_slots, (1, 0, 2)).reshape(source_slots, -1)
    live = jnp.arange(source_slots, dtype=jnp.int32) < plan_lengths[myself]
    row_grad, row_div = divergence(hidden_rows, teacher_slots, live, head_weight)
    column_of = (inverse - own_offset) % shards
    div_out = jnp.take(row_div.reshape(slot_depth, shards), column_of, axis=1, mode="clip").T
    div_in = lax.all_to_all(div_out, "dp", split_axis=0, concat_axis=0, tiled=True)
    packed = jnp.arange(balanced, dtype=jnp.int32) * shards + inverse[myself]
    owner = jnp.sum((offsets[None, :] <= packed[:, None]).astype(jnp.int32), axis=1) - 1
    row_kl = div_in[owner, (packed - offsets[owner]) // shards]
    return row_grad, row_kl


def solution(mesh):
    return jax.shard_map(
        body,
        mesh=mesh,
        in_specs=(P("dp", None), P(), P(), P(None, "vocab"), P("dp", "vocab")),
        out_specs=(P("dp", None), P("dp")),
        check_vma=False,
    )
```

```python
import jax
import jax.numpy as jnp
from jax import lax
from jax.sharding import PartitionSpec as P

loss_scale = 64.0


def divergence(row_block, teacher_block, live, weight):
    logits = jnp.dot(row_block, weight, preferred_element_type=jnp.float32)
    log_teacher = teacher_block.astype(jnp.float32)
    teacher_prob = jnp.exp(log_teacher)
    own_top = jnp.max(logits, axis=1)
    own_total = jnp.sum(jnp.exp(logits - own_top[:, None]), axis=1)
    own_mass = jnp.sum(teacher_prob, axis=1)
    own_cross = jnp.sum(teacher_prob * (log_teacher - logits), axis=1)
    stats = exchange_stats(jnp.stack([own_top, own_total, own_mass, own_cross]))
    tops, totals, masses, crosses = stats[:, 0], stats[:, 1], stats[:, 2], stats[:, 3]
    row_top = jnp.max(tops, axis=0)
    exp_total = jnp.sum(totals * jnp.exp(tops - row_top[None, :]), axis=0)
    prob_total = jnp.sum(masses, axis=0)
    cross_term = jnp.sum(crosses, axis=0)
    log_total = row_top + jnp.log(exp_total)
    row_div = jnp.where(live, cross_term + prob_total * log_total, 0.0)
    grad_logits = jnp.where(
        live[:, None],
        loss_scale * (prob_total[:, None] * jnp.exp(logits - log_total[:, None]) - teacher_prob),
        0.0,
    ).astype(jnp.bfloat16)
    partial_grad = lax.dot_general(
        grad_logits, weight, (((1,), (1,)), ((), ())), preferred_element_type=jnp.float32
    )
    hidden_grad = ring_all_reduce(partial_grad)
    return hidden_grad, row_div


def exchange_stats(local):
    ring = lax.axis_size("vocab")
    me = lax.axis_index("vocab")
    stats = jnp.broadcast_to(local[None], (ring,) + local.shape)
    slot = jnp.arange(ring, dtype=jnp.int32)[:, None, None]
    for off in range(1, ring):
        pairs = [(i, (i - off) % ring) for i in range(ring)]
        got = lax.ppermute(local, "vocab", pairs)
        stats = jnp.where(slot == (me + off) % ring, got[None], stats)
    return stats


def ring_all_reduce(partial):
    ring = lax.axis_size("vocab")
    me = lax.axis_index("vocab")
    rows, width = partial.shape
    chunk = rows // (2 * ring)
    halves = partial.reshape(2, ring, chunk, width)
    forward = [(i, (i + 1) % ring) for i in range(ring)]
    backward = [(i, (i - 1) % ring) for i in range(ring)]

    def own(half, index):
        return lax.dynamic_index_in_dim(halves[half], index % ring, 0, keepdims=False)

    up = own(0, me - 1)
    down = own(1, me + 1)
    for step in range(ring - 1):
        up = lax.ppermute(up, "vocab", forward)
        down = lax.ppermute(down, "vocab", backward)
        up = up + own(0, me - step - 2)
        down = down + own(1, me + step + 2)
    up = up.astype(jnp.bfloat16)
    down = down.astype(jnp.bfloat16)
    ups, downs = [up], [down]
    for _ in range(ring - 1):
        up = lax.ppermute(up, "vocab", forward)
        down = lax.ppermute(down, "vocab", backward)
        ups.append(up)
        downs.append(down)
    placed = jnp.zeros((2 * ring, chunk, width), jnp.bfloat16)
    for k in range(ring):
        placed = lax.dynamic_update_index_in_dim(placed, ups[k], (me - k) % ring, 0)
        placed = lax.dynamic_update_index_in_dim(placed, downs[k], ring + (me + k) % ring, 0)
    return placed.reshape(rows, width)


def body(hidden_rows, plan_lengths, shard_of_class, head_weight, teacher_logprobs):
    shards = lax.axis_size("dp")
    myself = lax.axis_index("dp")
    source_slots = hidden_rows.shape[0]
    slot_depth = source_slots // shards
    balanced = teacher_logprobs.shape[0]
    offsets = jnp.cumsum(plan_lengths) - plan_lengths
    classes = jnp.arange(shards, dtype=jnp.int32)
    inverse = jnp.sum(
        jnp.where(shard_of_class[None, :] == classes[:, None], classes[None, :], 0), axis=1
    )
    depth = jnp.arange(slot_depth, dtype=jnp.int32)
    first_col = (inverse[myself] - offsets) % shards
    first_slot = (offsets + first_col) // shards
    send_rows = jnp.minimum(first_slot[:, None] + depth[None, :], balanced - 1)
    outgoing = jnp.take(teacher_logprobs, send_rows, axis=0, mode="clip")
    arriving = lax.all_to_all(outgoing, "dp", split_axis=0, concat_axis=0, tiled=True)
    own_offset = offsets[myself]
    shard_at = shard_of_class[(own_offset + classes) % shards]
    teacher_slots = jnp.take(arriving, shard_at, axis=0, mode="clip")
    teacher_slots = jnp.transpose(teacher_slots, (1, 0, 2)).reshape(source_slots, -1)
    live = jnp.arange(source_slots, dtype=jnp.int32) < plan_lengths[myself]
    row_grad, row_div = divergence(hidden_rows, teacher_slots, live, head_weight)
    column_of = (inverse - own_offset) % shards
    div_out = jnp.take(row_div.reshape(slot_depth, shards), column_of, axis=1, mode="clip").T
    div_in = lax.all_to_all(div_out, "dp", split_axis=0, concat_axis=0, tiled=True)
    packed = jnp.arange(balanced, dtype=jnp.int32) * shards + inverse[myself]
    owner = jnp.sum((offsets[None, :] <= packed[:, None]).astype(jnp.int32), axis=1) - 1
    row_kl = div_in[owner, (packed - offsets[owner]) // shards]
    return row_grad, row_kl


def solution(mesh):
    return jax.shard_map(
        body,
        mesh=mesh,
        in_specs=(P("dp", None), P(), P(), P(None, "vocab"), P("dp", "vocab")),
        out_specs=(P("dp", None), P("dp")),
        check_vma=False,
    )
```

```python
import jax
import jax.numpy as jnp
from jax import lax
from jax.sharding import PartitionSpec as P

loss_scale = 64.0


def divergence(row_block, teacher_block, live, weight):
    logits = jnp.dot(row_block, weight, preferred_element_type=jnp.float32)
    log_teacher = teacher_block.astype(jnp.float32)
    teacher_prob = jnp.exp(log_teacher)
    own_top = jnp.max(logits, axis=1)
    own_total = jnp.sum(jnp.exp(logits - own_top[:, None]), axis=1)
    own_mass = jnp.sum(teacher_prob, axis=1)
    own_cross = jnp.sum(teacher_prob * (log_teacher - logits), axis=1)
    stats = exchange_stats(jnp.stack([own_top, own_total, own_mass, own_cross]))
    tops, totals, masses, crosses = stats[:, 0], stats[:, 1], stats[:, 2], stats[:, 3]
    row_top = jnp.max(tops, axis=0)
    exp_total = jnp.sum(totals * jnp.exp(tops - row_top[None, :]), axis=0)
    prob_total = jnp.sum(masses, axis=0)
    cross_term = jnp.sum(crosses, axis=0)
    log_total = row_top + jnp.log(exp_total)
    row_div = jnp.where(live, cross_term + prob_total * log_total, 0.0)
    grad_logits = jnp.where(
        live[:, None],
        loss_scale * (prob_total[:, None] * jnp.exp(logits - log_total[:, None]) - teacher_prob),
        0.0,
    ).astype(jnp.bfloat16)
    partial_grad = lax.dot_general(
        grad_logits, weight, (((1,), (1,)), ((), ())), preferred_element_type=jnp.float32
    )
    hidden_grad = ring_all_reduce(partial_grad)
    return hidden_grad, row_div


def exchange_stats(local):
    ring = lax.axis_size("vocab")
    me = lax.axis_index("vocab")
    stats = jnp.broadcast_to(local[None], (ring,) + local.shape)
    slot = jnp.arange(ring, dtype=jnp.int32)[:, None, None]
    for off in range(1, ring):
        pairs = [(i, (i - off) % ring) for i in range(ring)]
        got = lax.ppermute(local, "vocab", pairs)
        stats = jnp.where(slot == (me + off) % ring, got[None], stats)
    return stats


def ring_all_reduce(partial):
    ring = lax.axis_size("vocab")
    me = lax.axis_index("vocab")
    rows, width = partial.shape
    chunk = rows // (2 * ring)
    halves = partial.reshape(2, ring, chunk, width)
    forward = [(i, (i + 1) % ring) for i in range(ring)]
    backward = [(i, (i - 1) % ring) for i in range(ring)]

    def own(half, index):
        return lax.dynamic_index_in_dim(halves[half], index % ring, 0, keepdims=False)

    up = own(0, me - 1)
    down = own(1, me + 1)
    for step in range(ring - 1):
        up = lax.ppermute(up, "vocab", forward)
        down = lax.ppermute(down, "vocab", backward)
        up = up + own(0, me - step - 2)
        down = down + own(1, me + step + 2)
    up = up.astype(jnp.bfloat16)
    down = down.astype(jnp.bfloat16)
    ups, downs = [up], [down]
    for _ in range(ring - 1):
        up = lax.ppermute(up, "vocab", forward)
        down = lax.ppermute(down, "vocab", backward)
        ups.append(up)
        downs.append(down)
    placed = jnp.zeros((2 * ring, chunk, width), jnp.bfloat16)
    for k in range(ring):
        placed = lax.dynamic_update_index_in_dim(placed, ups[k], (me - k) % ring, 0)
        placed = lax.dynamic_update_index_in_dim(placed, downs[k], ring + (me + k) % ring, 0)
    return placed.reshape(rows, width)


def body(hidden_rows, plan_lengths, shard_of_class, head_weight, teacher_logprobs):
    shards = lax.axis_size("dp")
    myself = lax.axis_index("dp")
    source_slots = hidden_rows.shape[0]
    slot_depth = source_slots // shards
    balanced = teacher_logprobs.shape[0]
    offsets = jnp.cumsum(plan_lengths) - plan_lengths
    classes = jnp.arange(shards, dtype=jnp.int32)
    inverse = jnp.sum(
        jnp.where(shard_of_class[None, :] == classes[:, None], classes[None, :], 0), axis=1
    )
    depth = jnp.arange(slot_depth, dtype=jnp.int32)
    first_col = (inverse[myself] - offsets) % shards
    first_slot = (offsets + first_col) // shards
    send_rows = jnp.minimum(first_slot[:, None] + depth[None, :], balanced - 1)
    positions = jnp.arange(balanced, dtype=jnp.int32)
    selector = (send_rows.reshape(-1)[:, None] == positions[None, :]).astype(teacher_logprobs.dtype)
    outgoing = jnp.dot(selector, teacher_logprobs, preferred_element_type=jnp.float32)
    outgoing = outgoing.astype(teacher_logprobs.dtype)
    arriving = lax.all_to_all(outgoing, "dp", split_axis=0, concat_axis=0, tiled=True)
    own_offset = offsets[myself]
    shard_at = shard_of_class[(own_offset + classes) % shards]
    slot_source = (depth[:, None] + slot_depth * shard_at[None, :]).reshape(-1)
    picker = (slot_source[:, None] == jnp.arange(source_slots, dtype=jnp.int32)[None, :]).astype(arriving.dtype)
    teacher_slots = jnp.dot(picker, arriving, preferred_element_type=jnp.float32).astype(arriving.dtype)
    live = jnp.arange(source_slots, dtype=jnp.int32) < plan_lengths[myself]
    row_grad, row_div = divergence(hidden_rows, teacher_slots, live, head_weight)
    column_of = (inverse - own_offset) % shards
    div_out = jnp.take(row_div.reshape(slot_depth, shards), column_of, axis=1, mode="clip").T
    div_in = lax.all_to_all(div_out, "dp", split_axis=0, concat_axis=0, tiled=True)
    packed = jnp.arange(balanced, dtype=jnp.int32) * shards + inverse[myself]
    owner = jnp.sum((offsets[None, :] <= packed[:, None]).astype(jnp.int32), axis=1) - 1
    row_kl = div_in[owner, (packed - offsets[owner]) // shards]
    return row_grad, row_kl


def solution(mesh):
    return jax.shard_map(
        body,
        mesh=mesh,
        in_specs=(P("dp", None), P(), P(), P(None, "vocab"), P("dp", "vocab")),
        out_specs=(P("dp", None), P("dp")),
        check_vma=False,
    )
```

```python
import jax
import jax.numpy as jnp
from jax import lax
from jax.sharding import PartitionSpec as P

loss_scale = 64.0


def divergence(row_block, teacher_block, live, weight):
    logits = jnp.dot(row_block, weight, preferred_element_type=jnp.float32)
    log_teacher = teacher_block.astype(jnp.float32)
    teacher_prob = jnp.exp(log_teacher)
    own_top = jnp.max(logits, axis=1)
    own_total = jnp.sum(jnp.exp(logits - own_top[:, None]), axis=1)
    own_mass = jnp.sum(teacher_prob, axis=1)
    own_cross = jnp.sum(teacher_prob * (log_teacher - logits), axis=1)
    stats = exchange_stats(jnp.stack([own_top, own_total, own_mass, own_cross]))
    tops, totals, masses, crosses = stats[:, 0], stats[:, 1], stats[:, 2], stats[:, 3]
    row_top = jnp.max(tops, axis=0)
    exp_total = jnp.sum(totals * jnp.exp(tops - row_top[None, :]), axis=0)
    prob_total = jnp.sum(masses, axis=0)
    cross_term = jnp.sum(crosses, axis=0)
    log_total = row_top + jnp.log(exp_total)
    row_div = jnp.where(live, cross_term + prob_total * log_total, 0.0)
    grad_logits = jnp.where(
        live[:, None],
        loss_scale * (prob_total[:, None] * jnp.exp(logits - log_total[:, None]) - teacher_prob),
        0.0,
    ).astype(jnp.bfloat16)
    partial_grad = lax.dot_general(
        grad_logits, weight, (((1,), (1,)), ((), ())), preferred_element_type=jnp.float32
    )
    hidden_grad = ring_all_reduce(partial_grad)
    return hidden_grad, row_div


def exchange_stats(local):
    ring = lax.axis_size("vocab")
    me = lax.axis_index("vocab")
    stats = jnp.broadcast_to(local[None], (ring,) + local.shape)
    slot = jnp.arange(ring, dtype=jnp.int32)[:, None, None]
    for off in range(1, ring):
        pairs = [(i, (i - off) % ring) for i in range(ring)]
        got = lax.ppermute(local, "vocab", pairs)
        stats = jnp.where(slot == (me + off) % ring, got[None], stats)
    return stats


def ring_all_reduce(partial):
    ring = lax.axis_size("vocab")
    me = lax.axis_index("vocab")
    rows, width = partial.shape
    chunk = rows // (2 * ring)
    halves = partial.reshape(2, ring, chunk, width)
    forward = [(i, (i + 1) % ring) for i in range(ring)]
    backward = [(i, (i - 1) % ring) for i in range(ring)]

    def own(half, index):
        return lax.dynamic_index_in_dim(halves[half], index % ring, 0, keepdims=False)

    up = own(0, me - 1)
    down = own(1, me + 1)
    for step in range(ring - 1):
        up = lax.ppermute(up, "vocab", forward)
        down = lax.ppermute(down, "vocab", backward)
        up = up + own(0, me - step - 2)
        down = down + own(1, me + step + 2)
    up = up.astype(jnp.bfloat16)
    down = down.astype(jnp.bfloat16)
    ups, downs = [up], [down]
    for _ in range(ring - 1):
        up = lax.ppermute(up, "vocab", forward)
        down = lax.ppermute(down, "vocab", backward)
        ups.append(up)
        downs.append(down)
    placed = jnp.zeros((2 * ring, chunk, width), jnp.bfloat16)
    for k in range(ring):
        placed = lax.dynamic_update_index_in_dim(placed, ups[k], (me - k) % ring, 0)
        placed = lax.dynamic_update_index_in_dim(placed, downs[k], ring + (me + k) % ring, 0)
    return placed.reshape(rows, width)


def body(hidden_rows, plan_lengths, shard_of_class, head_weight, teacher_logprobs):
    shards = lax.axis_size("dp")
    myself = lax.axis_index("dp")
    source_slots = hidden_rows.shape[0]
    slot_depth = source_slots // shards
    balanced = teacher_logprobs.shape[0]
    offsets = jnp.cumsum(plan_lengths) - plan_lengths
    classes = jnp.arange(shards, dtype=jnp.int32)
    inverse = jnp.sum(
        jnp.where(shard_of_class[None, :] == classes[:, None], classes[None, :], 0), axis=1
    )
    depth = jnp.arange(slot_depth, dtype=jnp.int32)
    first_col = (inverse[myself] - offsets) % shards
    first_slot = (offsets + first_col) // shards
    send_rows = jnp.minimum(first_slot[:, None] + depth[None, :], balanced - 1)
    positions = jnp.arange(balanced, dtype=jnp.int32)
    selector = (send_rows.reshape(-1)[:, None] == positions[None, :]).astype(teacher_logprobs.dtype)
    outgoing = jnp.dot(selector, teacher_logprobs, preferred_element_type=jnp.float32)
    outgoing = outgoing.astype(teacher_logprobs.dtype)
    arriving = lax.all_to_all(outgoing, "dp", split_axis=0, concat_axis=0, tiled=True)
    own_offset = offsets[myself]
    shard_at = shard_of_class[(own_offset + classes) % shards]
    slot_source = (depth[:, None] + slot_depth * shard_at[None, :]).reshape(-1)
    picker = (slot_source[:, None] == jnp.arange(source_slots, dtype=jnp.int32)[None, :]).astype(arriving.dtype)
    teacher_slots = jnp.dot(picker, arriving, preferred_element_type=jnp.float32).astype(arriving.dtype)
    live = jnp.arange(source_slots, dtype=jnp.int32) < plan_lengths[myself]
    row_grad, row_div = divergence(hidden_rows, teacher_slots, live, head_weight)
    column_of = (inverse - own_offset) % shards
    div_out = jnp.take(row_div.reshape(slot_depth, shards), column_of, axis=1, mode="clip").T
    div_in = lax.all_to_all(div_out, "dp", split_axis=0, concat_axis=0, tiled=True)
    packed = jnp.arange(balanced, dtype=jnp.int32) * shards + inverse[myself]
    started = offsets[None, :] <= packed[:, None]
    owner = jnp.sum(started.astype(jnp.int32), axis=1) - 1
    owner_offset = jnp.max(jnp.where(started, offsets[None, :], 0), axis=1)
    flat = owner * slot_depth + (packed - owner_offset) // shards
    hit = flat[:, None] == jnp.arange(shards * slot_depth, dtype=jnp.int32)[None, :]
    row_kl = jnp.sum(jnp.where(hit, div_in.reshape(1, -1), 0.0), axis=1)
    return row_grad, row_kl


def solution(mesh):
    return jax.shard_map(
        body,
        mesh=mesh,
        in_specs=(P("dp", None), P(), P(), P(None, "vocab"), P("dp", "vocab")),
        out_specs=(P("dp", None), P("dp")),
        check_vma=False,
    )
```

```python
import jax
import jax.numpy as jnp
from jax import lax
from jax.sharding import PartitionSpec as P

loss_scale = 64.0


def divergence(row_block, teacher_block, live, weight):
    logits = jnp.dot(row_block, weight, preferred_element_type=jnp.float32)
    log_teacher = teacher_block.astype(jnp.float32)
    teacher_prob = jnp.exp(log_teacher)
    own_top = jnp.max(logits, axis=1)
    own_total = jnp.sum(jnp.exp(logits - own_top[:, None]), axis=1)
    own_mass = jnp.sum(teacher_prob, axis=1)
    own_cross = jnp.sum(teacher_prob * (log_teacher - logits), axis=1)
    stats = exchange_stats(jnp.stack([own_top, own_total, own_mass, own_cross]))
    tops, totals, masses, crosses = stats[:, 0], stats[:, 1], stats[:, 2], stats[:, 3]
    row_top = jnp.max(tops, axis=0)
    exp_total = jnp.sum(totals * jnp.exp(tops - row_top[None, :]), axis=0)
    prob_total = jnp.sum(masses, axis=0)
    cross_term = jnp.sum(crosses, axis=0)
    log_total = row_top + jnp.log(exp_total)
    row_div = jnp.where(live, cross_term + prob_total * log_total, 0.0)
    grad_logits = jnp.where(
        live[:, None],
        loss_scale * (prob_total[:, None] * jnp.exp(logits - log_total[:, None]) - teacher_prob),
        0.0,
    ).astype(jnp.bfloat16)
    partial_grad = lax.dot_general(
        grad_logits, weight, (((1,), (1,)), ((), ())), preferred_element_type=jnp.float32
    )
    hidden_grad = ring_all_reduce(partial_grad)
    return hidden_grad, row_div


def exchange_stats(local):
    ring = lax.axis_size("vocab")
    me = lax.axis_index("vocab")
    stats = jnp.broadcast_to(local[None], (ring,) + local.shape)
    slot = jnp.arange(ring, dtype=jnp.int32)[:, None, None]
    for off in range(1, ring):
        pairs = [(i, (i - off) % ring) for i in range(ring)]
        got = lax.ppermute(local, "vocab", pairs)
        stats = jnp.where(slot == (me + off) % ring, got[None], stats)
    return stats


def ring_all_reduce(partial):
    ring = lax.axis_size("vocab")
    me = lax.axis_index("vocab")
    rows, width = partial.shape
    chunk = rows // (2 * ring)
    halves = partial.reshape(2, ring, chunk, width)
    forward = [(i, (i + 1) % ring) for i in range(ring)]
    backward = [(i, (i - 1) % ring) for i in range(ring)]

    def own(half, index):
        return lax.dynamic_index_in_dim(halves[half], index % ring, 0, keepdims=False)

    up = own(0, me - 1)
    down = own(1, me + 1)
    for step in range(ring - 1):
        up = lax.ppermute(up, "vocab", forward)
        down = lax.ppermute(down, "vocab", backward)
        up = up + own(0, me - step - 2)
        down = down + own(1, me + step + 2)
    up = up.astype(jnp.bfloat16)
    down = down.astype(jnp.bfloat16)
    ups, downs = [up], [down]
    for _ in range(ring - 1):
        up = lax.ppermute(up, "vocab", forward)
        down = lax.ppermute(down, "vocab", backward)
        ups.append(up)
        downs.append(down)
    placed = jnp.zeros((2 * ring, chunk, width), jnp.bfloat16)
    for k in range(ring):
        placed = lax.dynamic_update_index_in_dim(placed, ups[k], (me - k) % ring, 0)
        placed = lax.dynamic_update_index_in_dim(placed, downs[k], ring + (me + k) % ring, 0)
    return placed.reshape(rows, width)


def body(hidden_rows, plan_lengths, shard_of_class, head_weight, teacher_logprobs):
    shards = lax.axis_size("dp")
    myself = lax.axis_index("dp")
    source_slots = hidden_rows.shape[0]
    slot_depth = source_slots // shards
    balanced = teacher_logprobs.shape[0]
    classes = jnp.arange(shards, dtype=jnp.int32)
    offsets = jnp.sum(jnp.where(classes[None, :] < classes[:, None], plan_lengths[None, :], 0), axis=1)
    inverse = jnp.sum(
        jnp.where(shard_of_class[None, :] == classes[:, None], classes[None, :], 0), axis=1
    )
    depth = jnp.arange(slot_depth, dtype=jnp.int32)
    first_col = (inverse[myself] - offsets) % shards
    first_slot = (offsets + first_col) // shards
    send_rows = jnp.minimum(first_slot[:, None] + depth[None, :], balanced - 1)
    positions = jnp.arange(balanced, dtype=jnp.int32)
    selector = (send_rows.reshape(-1)[:, None] == positions[None, :]).astype(teacher_logprobs.dtype)
    outgoing = jnp.dot(selector, teacher_logprobs, preferred_element_type=jnp.float32)
    outgoing = outgoing.astype(teacher_logprobs.dtype)
    arriving = lax.all_to_all(outgoing, "dp", split_axis=0, concat_axis=0, tiled=True)
    own_offset = offsets[myself]
    shard_at = shard_of_class[(own_offset + classes) % shards]
    slot_source = (depth[:, None] + slot_depth * shard_at[None, :]).reshape(-1)
    picker = (slot_source[:, None] == jnp.arange(source_slots, dtype=jnp.int32)[None, :]).astype(arriving.dtype)
    teacher_slots = jnp.dot(picker, arriving, preferred_element_type=jnp.float32).astype(arriving.dtype)
    live = jnp.arange(source_slots, dtype=jnp.int32) < plan_lengths[myself]
    row_grad, row_div = divergence(hidden_rows, teacher_slots, live, head_weight)
    column_of = (inverse - own_offset) % shards
    chosen = column_of[:, None, None] == classes[None, None, :]
    div_out = jnp.sum(jnp.where(chosen, row_div.reshape(1, slot_depth, shards), 0.0), axis=2)
    div_in = lax.all_to_all(div_out, "dp", split_axis=0, concat_axis=0, tiled=True)
    packed = jnp.arange(balanced, dtype=jnp.int32) * shards + inverse[myself]
    owner = jnp.sum((offsets[None, :] <= packed[:, None]).astype(jnp.int32), axis=1) - 1
    row_kl = div_in[owner, (packed - offsets[owner]) // shards]
    return row_grad, row_kl


def solution(mesh):
    return jax.shard_map(
        body,
        mesh=mesh,
        in_specs=(P("dp", None), P(), P(), P(None, "vocab"), P("dp", "vocab")),
        out_specs=(P("dp", None), P("dp")),
        check_vma=False,
    )
```
